512 devices in a mesh: replica: 32 (over x, y, core), tensor: 16 (over z).
Axes of the slice: x: 4, y: 4, z: 16, core: 2. Of those that a mesh axis runs over, the one named last changes fastest.
Arguments:
- hidden_first_step: bfloat16 [8192, 8192], P('replica', 'tensor'), may hold values from -6 to 6
- hidden_second_step: bfloat16 [8192, 8192], P('replica', 'tensor'), may hold values from -6 to 6
- value_matrix: bfloat16 [8192, 1024], P('tensor'), may hold values from -0.09375 to 0.09375
- down_maps: bfloat16 [256, 8192, 64], P('replica', 'tensor'), may hold values from -0.0625 to 0.0625
- up_maps: bfloat16 [256, 64, 1024], P('replica', None, 'tensor'), may hold values from -0.75 to 0.75
- adapter_storage_index: int32 [256], replicated, may hold values from 0 to 255, as said below
- adapter_of_group: int32 [128], P('replica'), may hold values from 0 to 255, as said below
Outputs:
- value_one: bfloat16 [8192, 1024], P('replica', 'tensor')
- value_two: bfloat16 [8192, 1024], P('replica', 'tensor')
The draws below stay inside these ranges and needn't reach their ends.
Inputs may be any that keep to these rules, and one draw needn't show every extreme that they name: A permutation: adapter a is stored at index adapter_storage_index[a] of down_maps and up_maps, that is on replica adapter_storage_index[a] // 8. Request rows g * 64 to (g + 1) * 64 - 1 use adapter adapter_of_group[g]. Among the 4 groups of one replica at most 1 use adapters stored on any one replica, and on every replica some storing replica serves exactly 1 of them. An adapter may serve several groups.
All inputs are finite; a program needn't handle non-finite values.
Results may differ from the reference program's by a relative error of at most 0.0036.
Values may be sent and summed in bfloat16 or wider, within the bound.
No kernel may reach another device: no remote copies, remote signals or barrier semaphores. Data moves between devices by JAX's collectives and lax.ppermute only.
A program may use at most 64 MiB of HBM per device.

```python
import jax
import jax.numpy as jnp
from jax import lax

MODEL_WIDTH = 8192
VALUE_OUTPUTS = 1024
ADAPTER_RANK = 64
G = 64
SEGS = 4
ADP_DEV = 8
CAP = 1
REQUESTS = 8192
ADAPTER_COUNT = 256
N_REPLICA = 32


def draw_adapter_storage_index(key, part):
    return jax.random.permutation(jax.random.fold_in(key, 11), ADAPTER_COUNT).astype(jnp.int32)


def draw_adapter_of_group(key, part):
    slot_of = draw_adapter_storage_index(key, part)
    inverse = jnp.argsort(slot_of).astype(jnp.int32)

    def one_replica(replica_key):
        key_one, key_two, key_three, key_four, key_five = jax.random.split(replica_key, 5)
        chosen_owner = jax.random.randint(key_one, (), 0, N_REPLICA)
        others = (chosen_owner + 1 + jnp.tile(jnp.arange(N_REPLICA - 1, dtype=jnp.int32), CAP)) % N_REPLICA
        others = jax.random.permutation(key_two, others)[:SEGS - CAP]
        owners = jnp.concatenate([jnp.full((CAP,), chosen_owner, dtype=jnp.int32), others.astype(jnp.int32)])
        owners = jax.random.permutation(key_three, owners)
        first_pick = jax.random.randint(key_four, (SEGS,), 0, ADP_DEV)
        second_pick = jax.random.randint(key_five, (SEGS,), 0, ADP_DEV)
        local_index = jnp.minimum(first_pick, second_pick)
        return inverse[owners * ADP_DEV + local_index]
    replica_keys = jax.random.split(jax.random.fold_in(key, 23), N_REPLICA)
    return jax.vmap(one_replica)(replica_keys).reshape(-1).astype(jnp.int32)


def with_spikes(entries, rng, source, target, shards_of, factor):
    owner, partner = [(jnp.arange(entries.shape[axis_at]) // (entries.shape[axis_at] // shards_of)).reshape([-1 if axis == axis_at else 1 for axis in range(entries.ndim)]) for axis_at in (source, target)]
    chosen = jax.random.permutation(rng, shards_of)[partner]
    strong = (owner == chosen) | (owner == (partner + shards_of // 2) % shards_of)
    return jnp.where(strong, factor * entries, entries)


def levels(stream_key, extent, pieces, smallest, high):
    factor_of = 1.0
    for position, shards_of in pieces:
        steps = jax.random.uniform(jax.random.fold_in(jax.random.fold_in(stream_key, 6), position), (shards_of,), jnp.float32, smallest / len(pieces), high / len(pieces))
        factor_of = factor_of * jnp.repeat(jnp.exp(steps), extent[position] // shards_of).reshape((-1,) + (1,) * (len(extent) - 1 - position))
    return factor_of


def centred(own_key, shape, scale, limit, cuts=(), kind=jnp.bfloat16):
    level = levels(own_key, shape, cuts, -0.22, 0.18) if cuts else 1.0
    entries = jax.random.normal(own_key, shape, jnp.float32) * scale * level
    return jnp.minimum(jnp.maximum(entries, -limit), limit).astype(kind)


def heavy_noise(rng, dims, deviation, reach, shards, heavy, kind=jnp.bfloat16):
    values = deviation * jax.random.normal(rng, dims, jnp.float32)
    if shards:
        values = values * levels(rng, dims, shards, -0.22, 0.18)
    return jnp.clip(with_spikes(values, jax.random.fold_in(rng, 3), *heavy), -reach, reach).astype(kind)


def setup_inputs(seed: int = 0) -> dict:
    seeds = jax.random.split(jax.random.key(seed), 8)
    hidden_first_step = centred(seeds[0], (REQUESTS, MODEL_WIDTH), 1.0, 6.0, ((0, 32), (1, 16)))
    hidden_second_step = centred(seeds[1], (REQUESTS, MODEL_WIDTH), 1.0, 6.0, ((0, 32), (1, 16)))
    value_matrix = heavy_noise(seeds[2], (MODEL_WIDTH, VALUE_OUTPUTS), MODEL_WIDTH ** -0.5, 0.09375, ((0, 16),), (0, 1, 16, 2.0))
    down_maps = centred(seeds[3], (ADAPTER_COUNT, MODEL_WIDTH, ADAPTER_RANK), MODEL_WIDTH ** -0.5, 0.0625, ((0, 32), (1, 16)))
    up_maps = centred(seeds[4], (ADAPTER_COUNT, ADAPTER_RANK, VALUE_OUTPUTS), ADAPTER_RANK ** -0.5, 0.75, ((0, 32), (2, 16)))
    adapter_storage_index = draw_adapter_storage_index(jax.random.fold_in(seeds[7], 71), 0)
    adapter_of_group = draw_adapter_of_group(jax.random.fold_in(seeds[7], 71), 0)
    return dict(hidden_first_step=hidden_first_step, hidden_second_step=hidden_second_step, value_matrix=value_matrix, down_maps=down_maps, up_maps=up_maps, adapter_storage_index=adapter_storage_index, adapter_of_group=adapter_of_group)


def reference(hidden_first_step, hidden_second_step, value_matrix, down_maps, up_maps, adapter_storage_index, adapter_of_group):
    slot_table = adapter_storage_index[adapter_of_group]
    weight_full = value_matrix.astype(jnp.float32)

    def one_replica(replica_index):
        storage_indices = lax.dynamic_slice_in_dim(slot_table, replica_index * SEGS, SEGS, 0)
        down_blocks = down_maps[storage_indices].astype(jnp.float32)
        up_blocks = up_maps[storage_indices].astype(jnp.float32)
        results = []
        for hidden in (hidden_first_step, hidden_second_step):
            hidden_rows = lax.dynamic_slice_in_dim(hidden, replica_index * (SEGS * G), SEGS * G, 0).astype(jnp.float32)
            base_sum = jnp.dot(hidden_rows, weight_full, precision=lax.Precision.HIGHEST)
            low_rank = jnp.einsum("sgd,sdr->sgr", hidden_rows.reshape(SEGS, G, MODEL_WIDTH), down_blocks, precision=lax.Precision.HIGHEST)
            low_rank = lax.optimization_barrier(low_rank.astype(jnp.bfloat16)).astype(jnp.float32)
            adapter_delta = jnp.einsum("sgr,src->sgc", low_rank, up_blocks, precision=lax.Precision.HIGHEST).reshape(SEGS * G, VALUE_OUTPUTS)
            results.append((base_sum + adapter_delta).astype(jnp.bfloat16))
        return results[0], results[1]

    first_step, second_step = lax.map(one_replica, jnp.arange(N_REPLICA, dtype=jnp.int32))
    return first_step.reshape(REQUESTS, VALUE_OUTPUTS), second_step.reshape(REQUESTS, VALUE_OUTPUTS)
```

```python
import jax
import jax.numpy as jnp
from jax import lax
from jax.sharding import PartitionSpec as P


def per_device(
    hidden_first_step,
    hidden_second_step,
    value_matrix,
    down_maps,
    up_maps,
    adapter_storage_index,
    adapter_of_group,
):
    replicas = lax.axis_size("replica")
    groups = adapter_of_group.shape[0]
    width_dev = hidden_first_step.shape[1]
    rank_extent = down_maps.shape[2]
    columns_per_replica = up_maps.shape[2]
    stored_adapters = down_maps.shape[0]
    row_count = hidden_first_step.shape[0]
    group_rows = row_count // groups

    slot_index = jnp.take(adapter_storage_index, adapter_of_group, axis=0)
    owners = slot_index // stored_adapters
    local_index = slot_index % stored_adapters
    owner_match = owners[:, None] == jnp.arange(replicas, dtype=jnp.int32)[None, :]
    wanted = jnp.sum(jnp.where(owner_match, local_index[:, None], 0), axis=0)

    base_one = jnp.dot(hidden_first_step, value_matrix, preferred_element_type=jnp.float32)
    base_two = jnp.dot(hidden_second_step, value_matrix, preferred_element_type=jnp.float32)
    summed_one = lax.psum_scatter(base_one, "tensor", scatter_dimension=1, tiled=True)
    summed_two = lax.psum_scatter(base_two, "tensor", scatter_dimension=1, tiled=True)

    requested = lax.all_to_all(
        wanted.reshape(replicas, 1), "replica", split_axis=0, concat_axis=0, tiled=True
    ).reshape(replicas)
    send_down = jnp.take(down_maps, requested, axis=0)
    send_up = jnp.take(up_maps, requested, axis=0)
    recv_down = lax.all_to_all(send_down, "replica", split_axis=0, concat_axis=0, tiled=True)
    recv_up = lax.all_to_all(send_up, "replica", split_axis=0, concat_axis=0, tiled=True)
    my_down = jnp.take(recv_down, owners, axis=0)
    my_up = jnp.take(recv_up, owners, axis=0)

    hidden_both = jnp.stack((hidden_first_step, hidden_second_step), axis=0).reshape(
        2, groups, group_rows, width_dev
    )
    low = jnp.einsum(
        "kgmw,gwr->kgmr", hidden_both, my_down, preferred_element_type=jnp.float32
    )
    low = lax.psum(low, "tensor").astype(jnp.bfloat16)
    delta = jnp.einsum("kgmr,grc->kgmc", low, my_up, preferred_element_type=jnp.float32)
    delta = delta.reshape(2, row_count, columns_per_replica)
    value_one = (summed_one + delta[0]).astype(jnp.bfloat16)
    value_two = (summed_two + delta[1]).astype(jnp.bfloat16)
    return (value_one, value_two)


def solution(mesh):
    return jax.shard_map(
        per_device,
        mesh=mesh,
        in_specs=(
            P("replica", "tensor"),
            P("replica", "tensor"),
            P("tensor", None),
            P("replica", "tensor", None),
            P("replica", None, "tensor"),
            P(),
            P("replica"),
        ),
        out_specs=(P("replica", "tensor"), P("replica", "tensor")),
        check_vma=False,
    )
```

```python
import jax
import jax.numpy as jnp
from jax import lax
from jax.sharding import PartitionSpec as P


def tensor_sum_bf16(partial):
    shards = lax.axis_size("tensor")
    pieces = partial.reshape(shards, partial.size // shards)
    pieces = lax.all_to_all(pieces, "tensor", split_axis=0, concat_axis=0, tiled=True)
    own = jnp.sum(pieces, axis=0, keepdims=True).astype(jnp.bfloat16)
    spread = jnp.broadcast_to(own, (shards, own.shape[1]))
    spread = lax.all_to_all(spread, "tensor", split_axis=0, concat_axis=0, tiled=True)
    return spread.reshape(partial.shape)


def per_device(
    hidden_first_step,
    hidden_second_step,
    value_matrix,
    down_maps,
    up_maps,
    adapter_storage_index,
    adapter_of_group,
):
    replicas = lax.axis_size("replica")
    groups = adapter_of_group.shape[0]
    width_dev = hidden_first_step.shape[1]
    rank_extent = down_maps.shape[2]
    columns_per_replica = up_maps.shape[2]
    stored_adapters = down_maps.shape[0]
    row_count = hidden_first_step.shape[0]
    group_rows = row_count // groups

    slot_index = jnp.take(adapter_storage_index, adapter_of_group, axis=0)
    owners = slot_index // stored_adapters
    local_index = slot_index % stored_adapters
    owner_match = owners[:, None] == jnp.arange(replicas, dtype=jnp.int32)[None, :]
    wanted = jnp.sum(jnp.where(owner_match, local_index[:, None], 0), axis=0)

    base_one = jnp.dot(hidden_first_step, value_matrix, preferred_element_type=jnp.float32)
    base_two = jnp.dot(hidden_second_step, value_matrix, preferred_element_type=jnp.float32)
    summed = lax.psum_scatter(
        jnp.stack((base_one, base_two), axis=0), "tensor", scatter_dimension=2, tiled=True
    )

    requested = lax.all_to_all(
        wanted.reshape(replicas, 1), "replica", split_axis=0, concat_axis=0, tiled=True
    ).reshape(replicas)
    send_down = jnp.take(down_maps, requested, axis=0)
    send_up = jnp.take(up_maps, requested, axis=0)
    recv_down = lax.all_to_all(send_down, "replica", split_axis=0, concat_axis=0, tiled=True)
    recv_up = lax.all_to_all(send_up, "replica", split_axis=0, concat_axis=0, tiled=True)
    my_down = jnp.take(recv_down, owners, axis=0)
    my_up = jnp.take(recv_up, owners, axis=0)

    hidden_both = jnp.stack((hidden_first_step, hidden_second_step), axis=0).reshape(
        2, groups, group_rows, width_dev
    )
    low = jnp.einsum(
        "kgmw,gwr->kgmr", hidden_both, my_down, preferred_element_type=jnp.float32
    )
    low = tensor_sum_bf16(low)
    delta = jnp.einsum("kgmr,grc->kgmc", low, my_up, preferred_element_type=jnp.float32)
    delta = delta.reshape(2, row_count, columns_per_replica)
    value_one = (summed[0] + delta[0]).astype(jnp.bfloat16)
    value_two = (summed[1] + delta[1]).astype(jnp.bfloat16)
    return (value_one, value_two)


def solution(mesh):
    return jax.shard_map(
        per_device,
        mesh=mesh,
        in_specs=(
            P("replica", "tensor"),
            P("replica", "tensor"),
            P("tensor", None),
            P("replica", "tensor", None),
            P("replica", None, "tensor"),
            P(),
            P("replica"),
        ),
        out_specs=(P("replica", "tensor"), P("replica", "tensor")),
        check_vma=False,
    )
```

```python
import jax
import jax.numpy as jnp
from jax import lax
from jax.sharding import PartitionSpec as P


def tensor_sum_bf16(partial):
    shards = lax.axis_size("tensor")
    pieces = partial.reshape(shards, partial.size // shards)
    pieces = lax.all_to_all(pieces, "tensor", split_axis=0, concat_axis=0, tiled=True)
    own = jnp.sum(pieces, axis=0, keepdims=True).astype(jnp.bfloat16)
    spread = jnp.broadcast_to(own, (shards, own.shape[1]))
    spread = lax.all_to_all(spread, "tensor", split_axis=0, concat_axis=0, tiled=True)
    return spread.reshape(partial.shape)


def per_device(
    hidden_first_step,
    hidden_second_step,
    value_matrix,
    down_maps,
    up_maps,
    adapter_storage_index,
    adapter_of_group,
):
    replicas = lax.axis_size("replica")
    groups = adapter_of_group.shape[0]
    width_dev = hidden_first_step.shape[1]
    rank_extent = down_maps.shape[2]
    columns_per_replica = up_maps.shape[2]
    stored_adapters = down_maps.shape[0]
    row_count = hidden_first_step.shape[0]
    group_rows = row_count // groups

    slot_index = jnp.take(adapter_storage_index, adapter_of_group, axis=0)
    owners = slot_index // stored_adapters
    local_index = slot_index % stored_adapters
    owner_match = owners[:, None] == jnp.arange(replicas, dtype=jnp.int32)[None, :]
    wanted = jnp.sum(jnp.where(owner_match, local_index[:, None], 0), axis=0)

    shards = lax.axis_size("tensor")
    hidden_pair = jnp.stack((hidden_first_step, hidden_second_step), axis=0)
    weight_blocks = value_matrix.reshape(width_dev, shards, value_matrix.shape[1] // shards)
    base = jnp.einsum(
        "rw,wtc->trc",
        hidden_pair.reshape(2 * row_count, width_dev),
        weight_blocks,
        preferred_element_type=jnp.float32,
    )
    summed = lax.psum_scatter(base, "tensor", scatter_dimension=0, tiled=True)
    summed = summed.reshape(2, row_count, columns_per_replica)

    requested = lax.all_to_all(
        wanted.reshape(replicas, 1), "replica", split_axis=0, concat_axis=0, tiled=True
    ).reshape(replicas)
    send_down = jnp.take(down_maps, requested, axis=0)
    send_up = jnp.take(up_maps, requested, axis=0)
    recv_down = lax.all_to_all(send_down, "replica", split_axis=0, concat_axis=0, tiled=True)
    recv_up = lax.all_to_all(send_up, "replica", split_axis=0, concat_axis=0, tiled=True)
    my_down = jnp.take(recv_down, owners, axis=0)
    my_up = jnp.take(recv_up, owners, axis=0)

    hidden_both = hidden_pair.reshape(2, groups, group_rows, width_dev)
    low = jnp.einsum(
        "kgmw,gwr->kgmr", hidden_both, my_down, preferred_element_type=jnp.float32
    )
    low = tensor_sum_bf16(low)
    delta = jnp.einsum("kgmr,grc->kgmc", low, my_up, preferred_element_type=jnp.float32)
    delta = delta.reshape(2, row_count, columns_per_replica)
    value_one = (summed[0] + delta[0]).astype(jnp.bfloat16)
    value_two = (summed[1] + delta[1]).astype(jnp.bfloat16)
    return (value_one, value_two)


def solution(mesh):
    return jax.shard_map(
        per_device,
        mesh=mesh,
        in_specs=(
            P("replica", "tensor"),
            P("replica", "tensor"),
            P("tensor", None),
            P("replica", "tensor", None),
            P("replica", None, "tensor"),
            P(),
            P("replica"),
        ),
        out_specs=(P("replica", "tensor"), P("replica", "tensor")),
        check_vma=False,
    )
```

```python
import jax
import jax.numpy as jnp
from jax import lax
from jax.sharding import PartitionSpec as P


def tensor_sum_bf16(partial):
    shards = lax.axis_size("tensor")
    pieces = partial.reshape(shards, partial.size // shards)
    pieces = lax.all_to_all(pieces, "tensor", split_axis=0, concat_axis=0, tiled=True)
    own = jnp.sum(pieces, axis=0, keepdims=True).astype(jnp.bfloat16)
    spread = jnp.broadcast_to(own, (shards, own.shape[1]))
    spread = lax.all_to_all(spread, "tensor", split_axis=0, concat_axis=0, tiled=True)
    return spread.reshape(partial.shape)


def per_device(
    hidden_first_step,
    hidden_second_step,
    value_matrix,
    down_maps,
    up_maps,
    adapter_storage_index,
    adapter_of_group,
):
    replicas = lax.axis_size("replica")
    groups = adapter_of_group.shape[0]
    width_dev = hidden_first_step.shape[1]
    rank_extent = down_maps.shape[2]
    columns_per_replica = up_maps.shape[2]
    stored_adapters = down_maps.shape[0]
    row_count = hidden_first_step.shape[0]
    group_rows = row_count // groups

    slot_index = jnp.take(adapter_storage_index, adapter_of_group, axis=0, mode="clip")
    owners = slot_index // stored_adapters
    local_index = slot_index % stored_adapters
    owner_match = owners[:, None] == jnp.arange(replicas, dtype=jnp.int32)[None, :]
    wanted = jnp.sum(jnp.where(owner_match, local_index[:, None], 0), axis=0)

    shards = lax.axis_size("tensor")
    hidden_pair = jnp.stack((hidden_first_step, hidden_second_step), axis=0)
    weight_blocks = value_matrix.reshape(width_dev, shards, value_matrix.shape[1] // shards)
    base = jnp.einsum(
        "rw,wtc->trc",
        hidden_pair.reshape(2 * row_count, width_dev),
        weight_blocks,
        preferred_element_type=jnp.float32,
    )
    summed = lax.psum_scatter(base, "tensor", scatter_dimension=0, tiled=True)
    summed = summed.reshape(2, row_count, columns_per_replica)

    requested = lax.all_to_all(
        wanted.reshape(replicas, 1), "replica", split_axis=0, concat_axis=0, tiled=True
    ).reshape(replicas)
    if rank_extent == columns_per_replica:
        maps = jnp.concatenate((down_maps, up_maps), axis=1)
        send_maps = jnp.take(maps, requested, axis=0, mode="clip")
        recv_maps = lax.all_to_all(send_maps, "replica", split_axis=0, concat_axis=0, tiled=True)
        my_maps = jnp.take(recv_maps, owners, axis=0, mode="clip")
        my_down = my_maps[:, :width_dev]
        my_up = my_maps[:, width_dev:]
    else:
        send_down = jnp.take(down_maps, requested, axis=0, mode="clip")
        send_up = jnp.take(up_maps, requested, axis=0, mode="clip")
        recv_down = lax.all_to_all(send_down, "replica", split_axis=0, concat_axis=0, tiled=True)
        recv_up = lax.all_to_all(send_up, "replica", split_axis=0, concat_axis=0, tiled=True)
        my_down = jnp.take(recv_down, owners, axis=0, mode="clip")
        my_up = jnp.take(recv_up, owners, axis=0, mode="clip")

    hidden_both = hidden_pair.reshape(2, groups, group_rows, width_dev)
    low = jnp.einsum(
        "kgmw,gwr->kgmr", hidden_both, my_down, preferred_element_type=jnp.float32
    )
    low = tensor_sum_bf16(low)
    delta = jnp.einsum("kgmr,grc->kgmc", low, my_up, preferred_element_type=jnp.float32)
    delta = delta.reshape(2, row_count, columns_per_replica)
    value_one = (summed[0] + delta[0]).astype(jnp.bfloat16)
    value_two = (summed[1] + delta[1]).astype(jnp.bfloat16)
    return (value_one, value_two)


def solution(mesh):
    return jax.shard_map(
        per_device,
        mesh=mesh,
        in_specs=(
            P("replica", "tensor"),
            P("replica", "tensor"),
            P("tensor", None),
            P("replica", "tensor", None),
            P("replica", None, "tensor"),
            P(),
            P("replica"),
        ),
        out_specs=(P("replica", "tensor"), P("replica", "tensor")),
        check_vma=False,
    )
```

```python
import jax
import jax.numpy as jnp
from jax import lax
from jax.sharding import PartitionSpec as P


def tensor_sum_bf16(partial):
    shards = lax.axis_size("tensor")
    pieces = partial.reshape(shards, partial.size // shards)
    pieces = lax.all_to_all(pieces, "tensor", split_axis=0, concat_axis=0, tiled=True)
    own = jnp.sum(pieces, axis=0, keepdims=True).astype(jnp.bfloat16)
    spread = jnp.broadcast_to(own, (shards, own.shape[1]))
    spread = lax.all_to_all(spread, "tensor", split_axis=0, concat_axis=0, tiled=True)
    return spread.reshape(partial.shape)


def per_device(
    hidden_first_step,
    hidden_second_step,
    value_matrix,
    down_maps,
    up_maps,
    adapter_storage_index,
    adapter_of_group,
):
    replicas = lax.axis_size("replica")
    groups = adapter_of_group.shape[0]
    width_dev = hidden_first_step.shape[1]
    rank_extent = down_maps.shape[2]
    columns_per_replica = up_maps.shape[2]
    stored_adapters = down_maps.shape[0]
    row_count = hidden_first_step.shape[0]
    group_rows = row_count // groups

    slot_index = jnp.take(adapter_storage_index, adapter_of_group, axis=0, mode="clip")
    owners = slot_index // stored_adapters
    local_index = slot_index % stored_adapters
    owner_match = owners[:, None] == jnp.arange(replicas, dtype=jnp.int32)[None, :]
    wanted = jnp.sum(jnp.where(owner_match, local_index[:, None], 0), axis=0)

    shards = lax.axis_size("tensor")
    hidden_pair = jnp.stack((hidden_first_step, hidden_second_step), axis=0)
    weight_blocks = value_matrix.reshape(width_dev, shards, value_matrix.shape[1] // shards)
    base = jnp.einsum(
        "rw,wtc->trc",
        hidden_pair.reshape(2 * row_count, width_dev),
        weight_blocks,
        preferred_element_type=jnp.float32,
    )
    summed = lax.psum_scatter(base, "tensor", scatter_dimension=0, tiled=True)
    summed = summed.reshape(2, row_count, columns_per_replica)

    requested = lax.all_to_all(
        wanted.reshape(replicas, 1), "replica", split_axis=0, concat_axis=0, tiled=True
    ).reshape(replicas)
    if rank_extent == columns_per_replica:
        maps = jnp.concatenate((down_maps, up_maps), axis=1)
        send_maps = jnp.take(maps, requested, axis=0, mode="clip")
        recv_maps = lax.all_to_all(send_maps, "replica", split_axis=0, concat_axis=0, tiled=True)
        my_maps = jnp.stack(
            [lax.dynamic_index_in_dim(recv_maps, owners[g], 0, keepdims=False) for g in range(groups)]
        )
        my_down = my_maps[:, :width_dev]
        my_up = my_maps[:, width_dev:]
    else:
        send_down = jnp.take(down_maps, requested, axis=0, mode="clip")
        send_up = jnp.take(up_maps, requested, axis=0, mode="clip")
        recv_down = lax.all_to_all(send_down, "replica", split_axis=0, concat_axis=0, tiled=True)
        recv_up = lax.all_to_all(send_up, "replica", split_axis=0, concat_axis=0, tiled=True)
        my_down = jnp.take(recv_down, owners, axis=0, mode="clip")
        my_up = jnp.take(recv_up, owners, axis=0, mode="clip")

    hidden_both = hidden_pair.reshape(2, groups, group_rows, width_dev)
    low = jnp.einsum(
        "kgmw,gwr->kgmr", hidden_both, my_down, preferred_element_type=jnp.float32
    )
    low = tensor_sum_bf16(low)
    delta = jnp.einsum("kgmr,grc->kgmc", low, my_up, preferred_element_type=jnp.float32)
    delta = delta.reshape(2, row_count, columns_per_replica)
    value_one = (summed[0] + delta[0]).astype(jnp.bfloat16)
    value_two = (summed[1] + delta[1]).astype(jnp.bfloat16)
    return (value_one, value_two)


def solution(mesh):
    return jax.shard_map(
        per_device,
        mesh=mesh,
        in_specs=(
            P("replica", "tensor"),
            P("replica", "tensor"),
            P("tensor", None),
            P("replica", "tensor", None),
            P("replica", None, "tensor"),
            P(),
            P("replica"),
        ),
        out_specs=(P("replica", "tensor"), P("replica", "tensor")),
        check_vma=False,
    )
```

```python
import jax
import jax.numpy as jnp
from jax import lax
from jax.sharding import PartitionSpec as P


def tensor_sum_bf16(partial):
    shards = lax.axis_size("tensor")
    pieces = partial.reshape(shards, partial.size // shards)
    pieces = lax.all_to_all(pieces, "tensor", split_axis=0, concat_axis=0, tiled=True)
    own = jnp.sum(pieces, axis=0, keepdims=True).astype(jnp.bfloat16)
    spread = jnp.broadcast_to(own, (shards, own.shape[1]))
    spread = lax.all_to_all(spread, "tensor", split_axis=0, concat_axis=0, tiled=True)
    return spread.reshape(partial.shape)


def per_device(
    hidden_first_step,
    hidden_second_step,
    value_matrix,
    down_maps,
    up_maps,
    adapter_storage_index,
    adapter_of_group,
):
    replicas = lax.axis_size("replica")
    groups = adapter_of_group.shape[0]
    width_dev = hidden_first_step.shape[1]
    rank_extent = down_maps.shape[2]
    columns_per_replica = up_maps.shape[2]
    stored_adapters = down_maps.shape[0]
    row_count = hidden_first_step.shape[0]
    group_rows = row_count // groups

    slot_index = jnp.take(adapter_storage_index, adapter_of_group, axis=0, mode="clip")
    owners = slot_index // stored_adapters
    local_index = slot_index % stored_adapters
    owner_match = owners[:, None] == jnp.arange(replicas, dtype=jnp.int32)[None, :]
    wanted = jnp.sum(jnp.where(owner_match, local_index[:, None], 0), axis=0)

    shards = lax.axis_size("tensor")
    hidden_pair = jnp.stack((hidden_first_step, hidden_second_step), axis=0)
    weight_blocks = value_matrix.reshape(width_dev, shards, value_matrix.shape[1] // shards)
    base = jnp.einsum(
        "rw,wtc->trc",
        hidden_pair.reshape(2 * row_count, width_dev),
        weight_blocks,
        preferred_element_type=jnp.float32,
    )
    summed = lax.psum_scatter(base, "tensor", scatter_dimension=0, tiled=True)
    summed = summed.reshape(2, row_count, columns_per_replica)

    requested = lax.all_to_all(
        wanted.reshape(replicas, 1), "replica", split_axis=0, concat_axis=0, tiled=True
    ).reshape(replicas)
    lanes = 128
    down_size = width_dev * rank_extent
    up_size = rank_extent * columns_per_replica
    if down_size % lanes == 0 and up_size % lanes == 0:
        down_rows = jnp.swapaxes(down_maps, 1, 2).reshape(stored_adapters, down_size // lanes, lanes)
        up_rows = up_maps.reshape(stored_adapters, up_size // lanes, lanes)
        maps = jnp.concatenate((down_rows, up_rows), axis=1)
        send_maps = jnp.take(maps, requested, axis=0, mode="clip")
        recv_maps = lax.all_to_all(send_maps, "replica", split_axis=0, concat_axis=0, tiled=True)
        my_maps = jnp.stack(
            [lax.dynamic_index_in_dim(recv_maps, owners[g], 0, keepdims=False) for g in range(groups)]
        )
        my_down = jnp.swapaxes(
            my_maps[:, : down_size // lanes].reshape(groups, rank_extent, width_dev), 1, 2
        )
        my_up = my_maps[:, down_size // lanes :].reshape(groups, rank_extent, columns_per_replica)
    else:
        send_down = jnp.take(down_maps, requested, axis=0, mode="clip")
        send_up = jnp.take(up_maps, requested, axis=0, mode="clip")
        recv_down = lax.all_to_all(send_down, "replica", split_axis=0, concat_axis=0, tiled=True)
        recv_up = lax.all_to_all(send_up, "replica", split_axis=0, concat_axis=0, tiled=True)
        my_down = jnp.take(recv_down, owners, axis=0, mode="clip")
        my_up = jnp.take(recv_up, owners, axis=0, mode="clip")

    hidden_both = hidden_pair.reshape(2, groups, group_rows, width_dev)
    low = jnp.einsum(
        "kgmw,gwr->kgmr", hidden_both, my_down, preferred_element_type=jnp.float32
    )
    low = tensor_sum_bf16(low)
    delta = jnp.einsum("kgmr,grc->kgmc", low, my_up, preferred_element_type=jnp.float32)
    delta = delta.reshape(2, row_count, columns_per_replica)
    value_one = (summed[0] + delta[0]).astype(jnp.bfloat16)
    value_two = (summed[1] + delta[1]).astype(jnp.bfloat16)
    return (value_one, value_two)


def solution(mesh):
    return jax.shard_map(
        per_device,
        mesh=mesh,
        in_specs=(
            P("replica", "tensor"),
            P("replica", "tensor"),
            P("tensor", None),
            P("replica", "tensor", None),
            P("replica", None, "tensor"),
            P(),
            P("replica"),
        ),
        out_specs=(P("replica", "tensor"), P("replica", "tensor")),
        check_vma=False,
    )
```

```python
import jax
import jax.numpy as jnp
from jax import lax
from jax.sharding import PartitionSpec as P


def tensor_sum_bf16(partial):
    shards = lax.axis_size("tensor")
    pieces = partial.reshape(shards, partial.size // shards).astype(jnp.bfloat16)
    pieces = lax.all_to_all(pieces, "tensor", split_axis=0, concat_axis=0, tiled=True)
    own = jnp.sum(pieces.astype(jnp.float32), axis=0, keepdims=True).astype(jnp.bfloat16)
    spread = jnp.broadcast_to(own, (shards, own.shape[1]))
    spread = lax.all_to_all(spread, "tensor", split_axis=0, concat_axis=0, tiled=True)
    return spread.reshape(partial.shape)


def per_device(
    hidden_first_step,
    hidden_second_step,
    value_matrix,
    down_maps,
    up_maps,
    adapter_storage_index,
    adapter_of_group,
):
    replicas = lax.axis_size("replica")
    groups = adapter_of_group.shape[0]
    width_dev = hidden_first_step.shape[1]
    rank_extent = down_maps.shape[2]
    columns_per_replica = up_maps.shape[2]
    stored_adapters = down_maps.shape[0]
    row_count = hidden_first_step.shape[0]
    group_rows = row_count // groups

    slot_index = jnp.take(adapter_storage_index, adapter_of_group, axis=0, mode="clip")
    owners = slot_index // stored_adapters
    local_index = slot_index % stored_adapters
    owner_match = owners[:, None] == jnp.arange(replicas, dtype=jnp.int32)[None, :]
    wanted = jnp.sum(jnp.where(owner_match, local_index[:, None], 0), axis=0)

    shards = lax.axis_size("tensor")
    hidden_pair = jnp.stack((hidden_first_step, hidden_second_step), axis=0)
    weight_blocks = value_matrix.reshape(width_dev, shards, value_matrix.shape[1] // shards)
    base = jnp.einsum(
        "rw,wtc->trc",
        hidden_pair.reshape(2 * row_count, width_dev),
        weight_blocks,
        preferred_element_type=jnp.float32,
    )
    summed = lax.psum_scatter(base, "tensor", scatter_dimension=0, tiled=True)
    summed = summed.reshape(2, row_count, columns_per_replica)

    requested = lax.all_to_all(
        wanted.reshape(replicas, 1), "replica", split_axis=0, concat_axis=0, tiled=True
    ).reshape(replicas)
    lanes = 128
    down_size = width_dev * rank_extent
    up_size = rank_extent * columns_per_replica
    if down_size % lanes == 0 and up_size % lanes == 0:
        down_rows = jnp.swapaxes(down_maps, 1, 2).reshape(stored_adapters, down_size // lanes, lanes)
        up_rows = up_maps.reshape(stored_adapters, up_size // lanes, lanes)
        maps = jnp.concatenate((down_rows, up_rows), axis=1)
        send_maps = jnp.take(maps, requested, axis=0, mode="clip")
        recv_maps = lax.all_to_all(send_maps, "replica", split_axis=0, concat_axis=0, tiled=True)
        my_maps = jnp.stack(
            [lax.dynamic_index_in_dim(recv_maps, owners[g], 0, keepdims=False) for g in range(groups)]
        )
        my_down = jnp.swapaxes(
            my_maps[:, : down_size // lanes].reshape(groups, rank_extent, width_dev), 1, 2
        )
        my_up = my_maps[:, down_size // lanes :].reshape(groups, rank_extent, columns_per_replica)
    else:
        send_down = jnp.take(down_maps, requested, axis=0, mode="clip")
        send_up = jnp.take(up_maps, requested, axis=0, mode="clip")
        recv_down = lax.all_to_all(send_down, "replica", split_axis=0, concat_axis=0, tiled=True)
        recv_up = lax.all_to_all(send_up, "replica", split_axis=0, concat_axis=0, tiled=True)
        my_down = jnp.take(recv_down, owners, axis=0, mode="clip")
        my_up = jnp.take(recv_up, owners, axis=0, mode="clip")

    hidden_both = hidden_pair.reshape(2, groups, group_rows, width_dev)
    low = jnp.einsum(
        "kgmw,gwr->kgmr", hidden_both, my_down, preferred_element_type=jnp.float32
    )
    low = tensor_sum_bf16(low)
    delta = jnp.einsum("kgmr,grc->kgmc", low, my_up, preferred_element_type=jnp.float32)
    delta = delta.reshape(2, row_count, columns_per_replica)
    value_one = (summed[0] + delta[0]).astype(jnp.bfloat16)
    value_two = (summed[1] + delta[1]).astype(jnp.bfloat16)
    return (value_one, value_two)


def solution(mesh):
    return jax.shard_map(
        per_device,
        mesh=mesh,
        in_specs=(
            P("replica", "tensor"),
            P("replica", "tensor"),
            P("tensor", None),
            P("replica", "tensor", None),
            P("replica", None, "tensor"),
            P(),
            P("replica"),
        ),
        out_specs=(P("replica", "tensor"), P("replica", "tensor")),
        check_vma=False,
    )
```

```python
import jax
import jax.numpy as jnp
from jax import lax
from jax.sharding import PartitionSpec as P


def tensor_sum_bf16(partial):
    shards = lax.axis_size("tensor")
    pieces = partial.reshape(shards, partial.size // shards)
    pieces = lax.all_to_all(pieces, "tensor", split_axis=0, concat_axis=0, tiled=True)
    own = jnp.sum(pieces, axis=0, keepdims=True).astype(jnp.bfloat16)
    spread = jnp.broadcast_to(own, (shards, own.shape[1]))
    spread = lax.all_to_all(spread, "tensor", split_axis=0, concat_axis=0, tiled=True)
    return spread.reshape(partial.shape)


def per_device(
    hidden_first_step,
    hidden_second_step,
    value_matrix,
    down_maps,
    up_maps,
    adapter_storage_index,
    adapter_of_group,
):
    replicas = lax.axis_size("replica")
    groups = adapter_of_group.shape[0]
    width_dev = hidden_first_step.shape[1]
    rank_extent = down_maps.shape[2]
    columns_per_replica = up_maps.shape[2]
    stored_adapters = down_maps.shape[0]
    row_count = hidden_first_step.shape[0]
    group_rows = row_count // groups

    table_size = adapter_storage_index.shape[0]
    adapter_match = adapter_of_group[:, None] == jnp.arange(table_size, dtype=jnp.int32)[None, :]
    slot_index = jnp.sum(jnp.where(adapter_match, adapter_storage_index[None, :], 0), axis=1)
    owners = slot_index // stored_adapters
    local_index = slot_index % stored_adapters
    owner_match = owners[:, None] == jnp.arange(replicas, dtype=jnp.int32)[None, :]
    wanted = jnp.sum(jnp.where(owner_match, local_index[:, None], 0), axis=0)

    shards = lax.axis_size("tensor")
    hidden_pair = jnp.stack((hidden_first_step, hidden_second_step), axis=0)
    weight_blocks = value_matrix.reshape(width_dev, shards, value_matrix.shape[1] // shards)
    base = jnp.einsum(
        "rw,wtc->trc",
        hidden_pair.reshape(2 * row_count, width_dev),
        weight_blocks,
        preferred_element_type=jnp.float32,
    )
    summed = lax.psum_scatter(base, "tensor", scatter_dimension=0, tiled=True)
    summed = summed.reshape(2, row_count, columns_per_replica)

    requested = lax.all_to_all(
        wanted.reshape(replicas, 1), "replica", split_axis=0, concat_axis=0, tiled=True
    ).reshape(replicas)
    lanes = 128
    down_size = width_dev * rank_extent
    up_size = rank_extent * columns_per_replica
    if down_size % lanes == 0 and up_size % lanes == 0:
        down_rows = jnp.swapaxes(down_maps, 1, 2).reshape(stored_adapters, down_size // lanes, lanes)
        up_rows = up_maps.reshape(stored_adapters, up_size // lanes, lanes)
        maps = jnp.concatenate((down_rows, up_rows), axis=1)
        send_maps = jnp.take(maps, requested, axis=0, mode="clip")
        recv_maps = lax.all_to_all(send_maps, "replica", split_axis=0, concat_axis=0, tiled=True)
        my_maps = jnp.stack(
            [lax.dynamic_index_in_dim(recv_maps, owners[g], 0, keepdims=False) for g in range(groups)]
        )
        my_down = jnp.swapaxes(
            my_maps[:, : down_size // lanes].reshape(groups, rank_extent, width_dev), 1, 2
        )
        my_up = my_maps[:, down_size // lanes :].reshape(groups, rank_extent, columns_per_replica)
    else:
        send_down = jnp.take(down_maps, requested, axis=0, mode="clip")
        send_up = jnp.take(up_maps, requested, axis=0, mode="clip")
        recv_down = lax.all_to_all(send_down, "replica", split_axis=0, concat_axis=0, tiled=True)
        recv_up = lax.all_to_all(send_up, "replica", split_axis=0, concat_axis=0, tiled=True)
        my_down = jnp.take(recv_down, owners, axis=0, mode="clip")
        my_up = jnp.take(recv_up, owners, axis=0, mode="clip")

    hidden_both = hidden_pair.reshape(2, groups, group_rows, width_dev)
    low = jnp.einsum(
        "kgmw,gwr->kgmr", hidden_both, my_down, preferred_element_type=jnp.float32
    )
    low = tensor_sum_bf16(low)
    delta = jnp.einsum("kgmr,grc->kgmc", low, my_up, preferred_element_type=jnp.float32)
    delta = delta.reshape(2, row_count, columns_per_replica)
    value_one = (summed[0] + delta[0]).astype(jnp.bfloat16)
    value_two = (summed[1] + delta[1]).astype(jnp.bfloat16)
    return (value_one, value_two)


def solution(mesh):
    return jax.shard_map(
        per_device,
        mesh=mesh,
        in_specs=(
            P("replica", "tensor"),
            P("replica", "tensor"),
            P("tensor", None),
            P("replica", "tensor", None),
            P("replica", None, "tensor"),
            P(),
            P("replica"),
        ),
        out_specs=(P("replica", "tensor"), P("replica", "tensor")),
        check_vma=False,
    )
```

```python
import jax
import jax.numpy as jnp
from jax import lax
from jax.sharding import PartitionSpec as P


def tensor_sum_bf16(partial):
    shards = lax.axis_size("tensor")
    pieces = partial.reshape(shards, partial.size // shards)
    pieces = lax.all_to_all(pieces, "tensor", split_axis=0, concat_axis=0, tiled=True)
    own = jnp.sum(pieces, axis=0, keepdims=True).astype(jnp.bfloat16)
    spread = jnp.broadcast_to(own, (shards, own.shape[1]))
    spread = lax.all_to_all(spread, "tensor", split_axis=0, concat_axis=0, tiled=True)
    return spread.reshape(partial.shape)


def per_device(
    hidden_first_step,
    hidden_second_step,
    value_matrix,
    down_maps,
    up_maps,
    adapter_storage_index,
    adapter_of_group,
):
    replicas = lax.axis_size("replica")
    groups = adapter_of_group.shape[0]
    width_dev = hidden_first_step.shape[1]
    rank_extent = down_maps.shape[2]
    columns_per_replica = up_maps.shape[2]
    stored_adapters = down_maps.shape[0]
    row_count = hidden_first_step.shape[0]
    group_rows = row_count // groups

    table_size = adapter_storage_index.shape[0]
    adapter_match = adapter_of_group[:, None] == jnp.arange(table_size, dtype=jnp.int32)[None, :]
    slot_index = jnp.sum(jnp.where(adapter_match, adapter_storage_index[None, :], 0), axis=1)
    owners = slot_index // stored_adapters
    local_index = slot_index % stored_adapters
    owner_match = owners[:, None] == jnp.arange(replicas, dtype=jnp.int32)[None, :]
    wanted = jnp.sum(jnp.where(owner_match, local_index[:, None], 0), axis=0)

    shards = lax.axis_size("tensor")
    hidden_pair = jnp.stack((hidden_first_step, hidden_second_step), axis=0)
    weight_blocks = value_matrix.reshape(width_dev, shards, value_matrix.shape[1] // shards)
    base = jnp.einsum(
        "rw,wtc->trc",
        hidden_pair.reshape(2 * row_count, width_dev),
        weight_blocks,
        preferred_element_type=jnp.float32,
    )
    summed = lax.psum_scatter(base, "tensor", scatter_dimension=0, tiled=True)
    summed = summed.reshape(2, row_count, columns_per_replica)

    requested = lax.all_to_all(
        wanted.reshape(replicas, 1), "replica", split_axis=0, concat_axis=0, tiled=True
    ).reshape(replicas)
    lanes = 128
    down_size = width_dev * rank_extent
    up_size = rank_extent * columns_per_replica
    if down_size % lanes == 0 and up_size % lanes == 0:
        down_rows = jnp.swapaxes(down_maps, 1, 2).reshape(stored_adapters, down_size // lanes, lanes)
        up_rows = up_maps.reshape(stored_adapters, up_size // lanes, lanes)
        maps = jnp.concatenate((down_rows, up_rows), axis=1)
        send_maps = jnp.take(maps, requested, axis=0, mode="clip")
        recv_maps = lax.all_to_all(send_maps, "replica", split_axis=0, concat_axis=0, tiled=True)
        picked = [lax.dynamic_index_in_dim(recv_maps, owners[g], 0, keepdims=False) for g in range(groups)]
        down_of = [m[: down_size // lanes].reshape(rank_extent, width_dev) for m in picked]
        my_up = jnp.stack(
            [m[down_size // lanes :].reshape(rank_extent, columns_per_replica) for m in picked]
        )
    else:
        send_down = jnp.take(down_maps, requested, axis=0, mode="clip")
        send_up = jnp.take(up_maps, requested, axis=0, mode="clip")
        recv_down = lax.all_to_all(send_down, "replica", split_axis=0, concat_axis=0, tiled=True)
        recv_up = lax.all_to_all(send_up, "replica", split_axis=0, concat_axis=0, tiled=True)
        my_down = jnp.take(recv_down, owners, axis=0, mode="clip")
        my_up = jnp.take(recv_up, owners, axis=0, mode="clip")

    hidden_both = hidden_pair.reshape(2, groups, group_rows, width_dev)
    if down_size % lanes == 0 and up_size % lanes == 0:
        low = jnp.stack(
            [
                jnp.einsum("kmw,rw->kmr", hidden_both[:, g], down_of[g], preferred_element_type=jnp.float32)
                for g in range(groups)
            ],
            axis=1,
        )
    else:
        low = jnp.einsum(
            "kgmw,gwr->kgmr", hidden_both, my_down, preferred_element_type=jnp.float32
        )
    low = tensor_sum_bf16(low)
    delta = jnp.einsum("kgmr,grc->kgmc", low, my_up, preferred_element_type=jnp.float32)
    delta = delta.reshape(2, row_count, columns_per_replica)
    value_one = (summed[0] + delta[0]).astype(jnp.bfloat16)
    value_two = (summed[1] + delta[1]).astype(jnp.bfloat16)
    return (value_one, value_two)


def solution(mesh):
    return jax.shard_map(
        per_device,
        mesh=mesh,
        in_specs=(
            P("replica", "tensor"),
            P("replica", "tensor"),
            P("tensor", None),
            P("replica", "tensor", None),
            P("replica", None, "tensor"),
            P(),
            P("replica"),
        ),
        out_specs=(P("replica", "tensor"), P("replica", "tensor")),
        check_vma=False,
    )
```

```python
import jax
import jax.numpy as jnp
from jax import lax
from jax.sharding import PartitionSpec as P


def tensor_sum_bf16(partial):
    shards = lax.axis_size("tensor")
    pieces = partial.reshape(shards, partial.size // shards)
    pieces = lax.all_to_all(pieces, "tensor", split_axis=0, concat_axis=0, tiled=True)
    own = jnp.sum(pieces, axis=0, keepdims=True).astype(jnp.bfloat16)
    spread = jnp.broadcast_to(own, (shards, own.shape[1]))
    spread = lax.all_to_all(spread, "tensor", split_axis=0, concat_axis=0, tiled=True)
    return spread.reshape(partial.shape)


def per_device(
    hidden_first_step,
    hidden_second_step,
    value_matrix,
    down_maps,
    up_maps,
    adapter_storage_index,
    adapter_of_group,
):
    replicas = lax.axis_size("replica")
    groups = adapter_of_group.shape[0]
    width_dev = hidden_first_step.shape[1]
    rank_extent = down_maps.shape[2]
    columns_per_replica = up_maps.shape[2]
    stored_adapters = down_maps.shape[0]
    row_count = hidden_first_step.shape[0]
    group_rows = row_count // groups

    table_size = adapter_storage_index.shape[0]
    adapter_match = adapter_of_group[:, None] == jnp.arange(table_size, dtype=jnp.int32)[None, :]
    slot_index = jnp.sum(jnp.where(adapter_match, adapter_storage_index[None, :], 0), axis=1)
    owners = slot_index // stored_adapters
    local_index = slot_index % stored_adapters
    owner_match = owners[:, None] == jnp.arange(replicas, dtype=jnp.int32)[None, :]
    wanted = jnp.sum(jnp.where(owner_match, local_index[:, None], 0), axis=0)

    shards = lax.axis_size("tensor")
    hidden_pair = jnp.stack((hidden_first_step, hidden_second_step), axis=0)
    weight_blocks = value_matrix.reshape(width_dev, shards, value_matrix.shape[1] // shards)
    base = jnp.einsum(
        "rw,wtc->trc",
        hidden_pair.reshape(2 * row_count, width_dev),
        weight_blocks,
        preferred_element_type=jnp.float32,
    )
    summed = lax.psum_scatter(base, "tensor", scatter_dimension=0, tiled=True)
    summed = summed.reshape(2 * row_count, columns_per_replica)

    requested = lax.all_to_all(
        wanted.reshape(replicas, 1), "replica", split_axis=0, concat_axis=0, tiled=True
    ).reshape(replicas)
    lanes = 128
    down_size = width_dev * rank_extent
    up_size = rank_extent * columns_per_replica
    if down_size % lanes == 0 and up_size % lanes == 0:
        down_rows = jnp.swapaxes(down_maps, 1, 2).reshape(stored_adapters, down_size // lanes, lanes)
        up_rows = up_maps.reshape(stored_adapters, up_size // lanes, lanes)
        maps = jnp.concatenate((down_rows, up_rows), axis=1)
        send_maps = jnp.take(maps, requested, axis=0, mode="clip")
        recv_maps = lax.all_to_all(send_maps, "replica", split_axis=0, concat_axis=0, tiled=True)
        my_maps = jnp.stack(
            [lax.dynamic_index_in_dim(recv_maps, owners[g], 0, keepdims=False) for g in range(groups)]
        )
        my_down = jnp.swapaxes(
            my_maps[:, : down_size // lanes].reshape(groups, rank_extent, width_dev), 1, 2
        )
        my_up = my_maps[:, down_size // lanes :].reshape(groups, rank_extent, columns_per_replica)
    else:
        send_down = jnp.take(down_maps, requested, axis=0, mode="clip")
        send_up = jnp.take(up_maps, requested, axis=0, mode="clip")
        recv_down = lax.all_to_all(send_down, "replica", split_axis=0, concat_axis=0, tiled=True)
        recv_up = lax.all_to_all(send_up, "replica", split_axis=0, concat_axis=0, tiled=True)
        my_down = jnp.take(recv_down, owners, axis=0, mode="clip")
        my_up = jnp.take(recv_up, owners, axis=0, mode="clip")

    hidden_both = hidden_pair.reshape(2, groups, group_rows, width_dev)
    low = jnp.einsum(
        "kgmw,gwr->kgmr", hidden_both, my_down, preferred_element_type=jnp.float32
    )
    low = tensor_sum_bf16(low)
    delta = jnp.einsum("kgmr,grc->kgmc", low, my_up, preferred_element_type=jnp.float32)
    delta = delta.reshape(2 * row_count, columns_per_replica)
    values = (summed + delta).astype(jnp.bfloat16)
    value_one = values[:row_count]
    value_two = values[row_count:]
    return (value_one, value_two)


def solution(mesh):
    return jax.shard_map(
        per_device,
        mesh=mesh,
        in_specs=(
            P("replica", "tensor"),
            P("replica", "tensor"),
            P("tensor", None),
            P("replica", "tensor", None),
            P("replica", None, "tensor"),
            P(),
            P("replica"),
        ),
        out_specs=(P("replica", "tensor"), P("replica", "tensor")),
        check_vma=False,
    )
```

```python
import jax
import jax.numpy as jnp
from jax import lax
from jax.sharding import PartitionSpec as P


def tensor_sum_bf16(partial):
    shards = lax.axis_size("tensor")
    lanes = 128
    share = partial.size // shards
    rows = share // lanes if share % lanes == 0 else 1
    pieces = partial.reshape(shards, rows, share // rows)
    pieces = lax.all_to_all(pieces, "tensor", split_axis=0, concat_axis=0, tiled=True)
    own = jnp.sum(pieces, axis=0, keepdims=True).astype(jnp.bfloat16)
    spread = jnp.broadcast_to(own, (shards,) + own.shape[1:])
    spread = lax.all_to_all(spread, "tensor", split_axis=0, concat_axis=0, tiled=True)
    return spread.reshape(partial.shape)


def per_device(
    hidden_first_step,
    hidden_second_step,
    value_matrix,
    down_maps,
    up_maps,
    adapter_storage_index,
    adapter_of_group,
):
    replicas = lax.axis_size("replica")
    groups = adapter_of_group.shape[0]
    width_dev = hidden_first_step.shape[1]
    rank_extent = down_maps.shape[2]
    columns_per_replica = up_maps.shape[2]
    stored_adapters = down_maps.shape[0]
    row_count = hidden_first_step.shape[0]
    group_rows = row_count // groups

    table_size = adapter_storage_index.shape[0]
    adapter_match = adapter_of_group[:, None] == jnp.arange(table_size, dtype=jnp.int32)[None, :]
    slot_index = jnp.sum(jnp.where(adapter_match, adapter_storage_index[None, :], 0), axis=1)
    owners = slot_index // stored_adapters
    local_index = slot_index % stored_adapters
    owner_match = owners[:, None] == jnp.arange(replicas, dtype=jnp.int32)[None, :]
    wanted = jnp.sum(jnp.where(owner_match, local_index[:, None], 0), axis=0)

    shards = lax.axis_size("tensor")
    hidden_pair = jnp.stack((hidden_first_step, hidden_second_step), axis=0)
    weight_blocks = value_matrix.reshape(width_dev, shards, value_matrix.shape[1] // shards)
    base = jnp.einsum(
        "rw,wtc->trc",
        hidden_pair.reshape(2 * row_count, width_dev),
        weight_blocks,
        preferred_element_type=jnp.float32,
    )
    summed = lax.psum_scatter(base, "tensor", scatter_dimension=0, tiled=True)
    summed = summed.reshape(2, row_count, columns_per_replica)

    requested = lax.all_to_all(
        wanted.reshape(replicas, 1), "replica", split_axis=0, concat_axis=0, tiled=True
    ).reshape(replicas)
    lanes = 128
    down_size = width_dev * rank_extent
    up_size = rank_extent * columns_per_replica
    if down_size % lanes == 0 and up_size % lanes == 0:
        down_rows = jnp.swapaxes(down_maps, 1, 2).reshape(stored_adapters, down_size // lanes, lanes)
        up_rows = up_maps.reshape(stored_adapters, up_size // lanes, lanes)
        maps = jnp.concatenate((down_rows, up_rows), axis=1)
        send_maps = jnp.take(maps, requested, axis=0, mode="clip")
        recv_maps = lax.all_to_all(send_maps, "replica", split_axis=0, concat_axis=0, tiled=True)
        my_maps = jnp.stack(
            [lax.dynamic_index_in_dim(recv_maps, owners[g], 0, keepdims=False) for g in range(groups)]
        )
        my_down = jnp.swapaxes(
            my_maps[:, : down_size // lanes].reshape(groups, rank_extent, width_dev), 1, 2
        )
        my_up = my_maps[:, down_size // lanes :].reshape(groups, rank_extent, columns_per_replica)
    else:
        send_down = jnp.take(down_maps, requested, axis=0, mode="clip")
        send_up = jnp.take(up_maps, requested, axis=0, mode="clip")
        recv_down = lax.all_to_all(send_down, "replica", split_axis=0, concat_axis=0, tiled=True)
        recv_up = lax.all_to_all(send_up, "replica", split_axis=0, concat_axis=0, tiled=True)
        my_down = jnp.take(recv_down, owners, axis=0, mode="clip")
        my_up = jnp.take(recv_up, owners, axis=0, mode="clip")

    hidden_both = hidden_pair.reshape(2, groups, group_rows, width_dev)
    low = jnp.einsum(
        "kgmw,gwr->kgmr", hidden_both, my_down, preferred_element_type=jnp.float32
    )
    low = tensor_sum_bf16(low)
    delta = jnp.einsum("kgmr,grc->kgmc", low, my_up, preferred_element_type=jnp.float32)
    delta = delta.reshape(2, row_count, columns_per_replica)
    value_one = (summed[0] + delta[0]).astype(jnp.bfloat16)
    value_two = (summed[1] + delta[1]).astype(jnp.bfloat16)
    return (value_one, value_two)


def solution(mesh):
    return jax.shard_map(
        per_device,
        mesh=mesh,
        in_specs=(
            P("replica", "tensor"),
            P("replica", "tensor"),
            P("tensor", None),
            P("replica", "tensor", None),
            P("replica", None, "tensor"),
            P(),
            P("replica"),
        ),
        out_specs=(P("replica", "tensor"), P("replica", "tensor")),
        check_vma=False,
    )
```

```python
import jax
import jax.numpy as jnp
from jax import lax
from jax.sharding import PartitionSpec as P


def tensor_sum_bf16(partial):
    shards = lax.axis_size("tensor")
    lanes = 128
    share = partial.size // shards
    rows = share // lanes if share % lanes == 0 else 1
    pieces = partial.reshape(shards, rows, share // rows)
    pieces = lax.all_to_all(pieces, "tensor", split_axis=0, concat_axis=0, tiled=True)
    own = jnp.sum(pieces, axis=0, keepdims=True).astype(jnp.bfloat16)
    spread = jnp.broadcast_to(own, (shards,) + own.shape[1:])
    spread = lax.all_to_all(spread, "tensor", split_axis=0, concat_axis=0, tiled=True)
    return spread.reshape(partial.shape)


def per_device(
    hidden_first_step,
    hidden_second_step,
    value_matrix,
    down_maps,
    up_maps,
    adapter_storage_index,
    adapter_of_group,
):
    replicas = lax.axis_size("replica")
    groups = adapter_of_group.shape[0]
    width_dev = hidden_first_step.shape[1]
    rank_extent = down_maps.shape[2]
    columns_per_replica = up_maps.shape[2]
    stored_adapters = down_maps.shape[0]
    row_count = hidden_first_step.shape[0]
    group_rows = row_count // groups

    table_size = adapter_storage_index.shape[0]
    adapter_match = adapter_of_group[:, None] == jnp.arange(table_size, dtype=jnp.int32)[None, :]
    slot_index = jnp.sum(jnp.where(adapter_match, adapter_storage_index[None, :], 0), axis=1)
    owners = slot_index // stored_adapters
    local_index = slot_index % stored_adapters
    owner_match = owners[:, None] == jnp.arange(replicas, dtype=jnp.int32)[None, :]
    wanted = jnp.sum(jnp.where(owner_match, local_index[:, None], 0), axis=0)

    shards = lax.axis_size("tensor")
    hidden_pair = jnp.stack((hidden_first_step, hidden_second_step), axis=0)
    weight_blocks = value_matrix.reshape(width_dev, shards, value_matrix.shape[1] // shards)
    base = jnp.einsum(
        "rw,wtc->trc",
        hidden_pair.reshape(2 * row_count, width_dev),
        weight_blocks,
        preferred_element_type=jnp.float32,
    )
    summed = lax.psum_scatter(base, "tensor", scatter_dimension=0, tiled=True)
    summed = summed.reshape(2, row_count, columns_per_replica)

    requested = lax.all_to_all(
        jnp.broadcast_to(wanted[:, None, None], (replicas, 1, 128)),
        "replica",
        split_axis=0,
        concat_axis=0,
        tiled=True,
    )[:, 0, 0]
    lanes = 128
    down_size = width_dev * rank_extent
    up_size = rank_extent * columns_per_replica
    if down_size % lanes == 0 and up_size % lanes == 0:
        down_rows = jnp.swapaxes(down_maps, 1, 2).reshape(stored_adapters, down_size // lanes, lanes)
        up_rows = up_maps.reshape(stored_adapters, up_size // lanes, lanes)
        maps = jnp.concatenate((down_rows, up_rows), axis=1)
        send_maps = jnp.take(maps, requested, axis=0, mode="clip")
        recv_maps = lax.all_to_all(send_maps, "replica", split_axis=0, concat_axis=0, tiled=True)
        my_maps = jnp.stack(
            [lax.dynamic_index_in_dim(recv_maps, owners[g], 0, keepdims=False) for g in range(groups)]
        )
        my_down = jnp.swapaxes(
            my_maps[:, : down_size // lanes].reshape(groups, rank_extent, width_dev), 1, 2
        )
        my_up = my_maps[:, down_size // lanes :].reshape(groups, rank_extent, columns_per_replica)
    else:
        send_down = jnp.take(down_maps, requested, axis=0, mode="clip")
        send_up = jnp.take(up_maps, requested, axis=0, mode="clip")
        recv_down = lax.all_to_all(send_down, "replica", split_axis=0, concat_axis=0, tiled=True)
        recv_up = lax.all_to_all(send_up, "replica", split_axis=0, concat_axis=0, tiled=True)
        my_down = jnp.take(recv_down, owners, axis=0, mode="clip")
        my_up = jnp.take(recv_up, owners, axis=0, mode="clip")

    hidden_both = hidden_pair.reshape(2, groups, group_rows, width_dev)
    low = jnp.einsum(
        "kgmw,gwr->kgmr", hidden_both, my_down, preferred_element_type=jnp.float32
    )
    low = tensor_sum_bf16(low)
    delta = jnp.einsum("kgmr,grc->kgmc", low, my_up, preferred_element_type=jnp.float32)
    delta = delta.reshape(2, row_count, columns_per_replica)
    value_one = (summed[0] + delta[0]).astype(jnp.bfloat16)
    value_two = (summed[1] + delta[1]).astype(jnp.bfloat16)
    return (value_one, value_two)


def solution(mesh):
    return jax.shard_map(
        per_device,
        mesh=mesh,
        in_specs=(
            P("replica", "tensor"),
            P("replica", "tensor"),
            P("tensor", None),
            P("replica", "tensor", None),
            P("replica", None, "tensor"),
            P(),
            P("replica"),
        ),
        out_specs=(P("replica", "tensor"), P("replica", "tensor")),
        check_vma=False,
    )
```
